512 devices in a mesh: node: 8 (over y, x_lo), space: 64 (over z, x_hi, core).
Axes of the slice: x: 4 (x_hi: 2, x_lo: 2; x = x_hi * 2 + x_lo), y: 4, z: 16, core: 2. Of those that a mesh axis runs over, the one named last changes fastest.
Arguments:
- grain_ids: int32 [256, 16, 128], P('space'), may hold values from 0 to 7
- peak_heat: float32 [256, 16, 128], P('space'), may hold values from 0.5 to 1
Outputs:
- node_states: float32 [8, 8, 256, 16, 128], P('node', None, 'space')
The draws below stay inside these ranges and needn't reach their ends.
All inputs are finite; a program needn't handle non-finite values.
Results may differ from the reference program's by a relative error of at most 0.0001.
Values sent between devices are 32-bit elements; how exact they have to be, the bound alone decides.
No kernel may reach another device: no remote copies, remote signals or barrier semaphores. Data moves between devices by JAX's collectives and lax.ppermute only.
A program may use at most 64 MiB of HBM per device.

```python
import math
import jax
import jax.numpy as jnp
import numpy as np
from jax import lax

P_SIZE = 8
NODES = 8
CX = 128
CY = 16
NZ = 256
SWEEPS = 3
JACOBI = 2
STEPS = 2


def with_ends(values, key, smallest, top_value):
    dims = values.shape
    spot = [jax.random.randint(jax.random.fold_in(key, axis), (), 0, dims[axis]) for axis in range(len(dims))]
    values = values.at[tuple(spot)].set(smallest)
    longest = dims.index(max(dims))
    spot[longest] = (spot[longest] + 1) % dims[longest]
    return values.at[tuple(spot)].set(top_value)


def block_scale(rng, shape, pieces, low, top_value):
    loudness = 1.0
    for position, blocks in pieces:
        draws = jax.random.uniform(jax.random.fold_in(jax.random.fold_in(rng, 6), position), (blocks,), jnp.float32, low / len(pieces), top_value / len(pieces))
        loudness = loudness * jnp.repeat(jnp.exp(draws), shape[position] // blocks).reshape((-1,) + (1,) * (len(shape) - 1 - position))
    return loudness


def setup_inputs(seed: int = 0) -> dict:
    splits = jax.random.split(jax.random.key(seed), 3)
    return {
        "grain_ids": with_ends(jax.random.randint(splits[0], (NZ, CY, CX), 0, P_SIZE), jax.random.fold_in(splits[0], 1), 0, P_SIZE - 1).astype(jnp.int32),
        "peak_heat": jnp.clip(0.5 + 0.5 * jax.random.uniform(splits[1], (NZ, CY, CX), jnp.float32) ** block_scale(splits[1], (NZ, CY, CX), ((0, 64),), -0.2, 0.2), 0.5, 1.0),
    }


time_step = 0.25
cross_coef = 1.5
base_heat = 0.45
activation = 3.0


def legendre_pair(count, point):
    before = 1.0
    current = point
    for degree in range(2, count + 1):
        following = ((2 * degree - 1) * point * current - (degree - 1) * before) / degree
        before = current
        current = following
    return current, before


def radau_value(count, point):
    high, low = legendre_pair(count, point)
    high_prev, low_prev = legendre_pair(count - 1, point) if count > 1 else (1.0, 1.0)
    value = high - low
    slope_high = count * (point * high - low) / (point * point - 1.0)
    if count > 1:
        slope_low = (count - 1) * (point * high_prev - low_prev) / (point * point - 1.0)
    else:
        slope_low = 0.0
    return value, slope_high - slope_low


def radau_table(count):
    roots = [1.0]
    for index in range(1, count):
        point = math.cos(2.0 * math.pi * index / (2 * count - 1))
        for repeat in range(100):
            value, slope = radau_value(count, point)
            point = point - value / slope
        roots.append(point)
    roots = sorted(roots)
    times_list = [(value + 1.0) / 2.0 for value in roots]
    times_list[-1] = 1.0
    table = []
    for row_index in range(count):
        upper = times_list[row_index]
        row_values = []
        for column in range(count):
            poly = [1.0]
            for other in range(count):
                if other != column:
                    scale = times_list[column] - times_list[other]
                    shifted = [0.0] + poly
                    scaled = [c * times_list[other] for c in poly] + [0.0]
                    poly = [(shifted[i] - scaled[i]) / scale for i in range(len(shifted))]
            integral_value = 0.0
            for power in range(len(poly)):
                integral_value += poly[power] * upper ** (power + 1) / (power + 1)
            row_values.append(integral_value)
        table.append(row_values)
    return np.array(times_list), np.array(table)


def drive(field):
    squares = field * field
    total = jnp.sum(squares, axis=-4, keepdims=True)
    return -field + squares * field + 2.0 * cross_coef * field * (total - squares)


def neighbours(field):
    result = jnp.roll(field, -1, -3) + jnp.roll(field, 1, -3)
    result = result + jnp.roll(field, -1, -2) + jnp.roll(field, 1, -2)
    return result + jnp.roll(field, -1, -1) + jnp.roll(field, 1, -1)


def heat_mobility(peak, moment):
    middle = 0.5 * time_step * STEPS
    theta = base_heat + (peak - base_heat) * jnp.exp(-((moment - middle) / middle) ** 2)
    return jnp.exp(activation * (1.0 - 1.0 / theta))


def rate(field, mobility):
    return -mobility * (drive(field) - (neighbours(field) - 6.0 * field))


def relax(field, goal, factor):
    return (goal + factor * (neighbours(field) - drive(field))) / (1.0 + 6.0 * factor)


def reference(grain_ids, peak_heat):
    node_times, table = radau_table(NODES)
    times = jnp.asarray(node_times, jnp.float32)
    weights = jnp.asarray(table, jnp.float32)
    orders = jnp.arange(P_SIZE, dtype=jnp.int32)
    start = (grain_ids[None] == orders[:, None, None, None]).astype(jnp.float32)
    taus = times.reshape((NODES, 1, 1, 1, 1))
    states = None
    for step_index in range(STEPS):
        moments = (step_index + times) * time_step
        mobility = heat_mobility(peak_heat[None], moments[:, None, None, None])[:, None]
        factor = time_step * taus * mobility
        rates = rate(start[None], mobility)
        states = jnp.broadcast_to(start[None], rates.shape)
        for sweep_index in range(SWEEPS):
            quad = jnp.tensordot(weights, rates, axes=1, precision=lax.Precision.HIGHEST)
            goal = start[None] + time_step * quad - time_step * taus * rates
            for relax_index in range(JACOBI):
                states = relax(states, goal, factor)
            if sweep_index + 1 < SWEEPS:
                rates = rate(states, mobility)
        start = states[-1]
    return states
```

```python
import functools
import math

import jax
import jax.numpy as jnp
import numpy as np
from jax import lax
from jax.experimental import pallas as pl
from jax.experimental.pallas import tpu as pltpu
from jax.sharding import PartitionSpec as P

P_SIZE = 8
NODE_DEV = 1
SWEEPS = 3
JACOBI = 2
STEPS = 2


time_step = 0.25
cross_coef = 1.5
base_heat = 0.45
activation = 3.0


def gather_halo(block, dim, width):
    axis = "space"
    count = lax.axis_size(axis)
    size = block.shape[dim]
    lows = []
    highs = []
    distance = 1
    left = width
    while left > 0:
        take = min(size, left)
        up = [(i, (i + distance) % count) for i in range(count)]
        down = [(i, (i - distance) % count) for i in range(count)]
        lows.insert(0, lax.ppermute(lax.slice_in_dim(block, size - take, size, axis=dim), axis, up))
        highs.append(lax.ppermute(lax.slice_in_dim(block, 0, take, axis=dim), axis, down))
        left -= take
        distance += 1
    return jnp.concatenate(lows + [block] + highs, axis=dim)


def trim(block, count, dim=-3):
    if count == 0:
        return block
    return lax.slice_in_dim(block, count, block.shape[dim] - count, axis=dim)


def legendre_pair(count, point):
    before = 1.0
    current = point
    for degree in range(2, count + 1):
        following = ((2 * degree - 1) * point * current - (degree - 1) * before) / degree
        before = current
        current = following
    return (current, before)


def radau_value(count, point):
    high, low = legendre_pair(count, point)
    high_prev, low_prev = legendre_pair(count - 1, point)
    value = high - low
    slope_high = count * (point * high - low) / (point * point - 1.0)
    slope_low = (count - 1) * (point * high_prev - low_prev) / (point * point - 1.0)
    return (value, slope_high - slope_low)


def radau_table(count):
    roots = [1.0]
    for index in range(1, count):
        point = math.cos(2.0 * math.pi * index / (2 * count - 1))
        for repeat in range(100):
            value, slope = radau_value(count, point)
            point = point - value / slope
        roots.append(point)
    roots = sorted(roots)
    times_list = [(value + 1.0) / 2.0 for value in roots]
    times_list[-1] = 1.0
    table = []
    for row_index in range(count):
        upper = times_list[row_index]
        row_values = []
        for column in range(count):
            poly = [1.0]
            for other in range(count):
                if other != column:
                    scale = times_list[column] - times_list[other]
                    shifted = [0.0] + poly
                    scaled = [c * times_list[other] for c in poly] + [0.0]
                    poly = [(shifted[i] - scaled[i]) / scale for i in range(len(shifted))]
            integral_value = 0.0
            for power in range(len(poly)):
                integral_value += poly[power] * upper ** (power + 1) / (power + 1)
            row_values.append(integral_value)
        table.append(row_values)
    return (np.array(times_list), np.array(table))


def drive(field):
    squares = field * field
    total = jnp.sum(squares, axis=-4, keepdims=True)
    return -field + squares * field + 2.0 * cross_coef * field * (total - squares)


def near_sum(extended):
    inner = extended[..., 1:-1, :, :]
    result = extended[..., 2:, :, :] + extended[..., :-2, :, :]
    result = result + jnp.roll(inner, -1, -2) + jnp.roll(inner, 1, -2)
    return result + jnp.roll(inner, -1, -1) + jnp.roll(inner, 1, -1)


def heat_mobility(peak, moment):
    middle = 0.5 * time_step * STEPS
    theta = base_heat + (peak - base_heat) * jnp.exp(-(((moment - middle) / middle) ** 2))
    return jnp.exp(activation * (1.0 - 1.0 / theta))


def rate_on(extended, mobility):
    inner = extended[..., 1:-1, :, :]
    return -mobility * (drive(inner) - (near_sum(extended) - 6.0 * inner))


def relax_on(extended, goal, factor):
    inner = extended[..., 1:-1, :, :]
    return (goal + factor * (near_sum(extended) - drive(inner))) / (1.0 + 6.0 * factor)


def plane_near(below, center, above):
    result = above + below
    result = result + pltpu.roll(center, center.shape[1] - 1, 1) + pltpu.roll(center, 1, 1)
    return result + pltpu.roll(center, center.shape[2] - 1, 2) + pltpu.roll(center, 1, 2)


def plane_drive(field):
    squares = field * field
    total = jnp.sum(squares, axis=0, keepdims=True)
    return -field + squares * field + 2.0 * cross_coef * field * (total - squares)


def prep_kernel(start_ref, bracket_ref, pull_ref):
    def body(z, carry):
        center = start_ref[:, z + 1]
        near = plane_near(start_ref[:, z], center, start_ref[:, z + 2])
        push = plane_drive(center)
        bracket_ref[:, z] = push - (near - 6.0 * center)
        pull_ref[:, z] = near - push
        return carry

    lax.fori_loop(0, bracket_ref.shape[1], body, 0)


def prep_call(start):
    count, planes, rows, lanes = start.shape
    shape = jax.ShapeDtypeStruct((count, planes - 2, rows, lanes), jnp.float32)
    return pl.pallas_call(
        prep_kernel,
        out_shape=(shape, shape),
        in_specs=[pl.BlockSpec(memory_space=pltpu.VMEM)],
        out_specs=(pl.BlockSpec(memory_space=pltpu.VMEM), pl.BlockSpec(memory_space=pltpu.VMEM)),
    )(start)


def sweep_kernel(
    sel_ref, coef_ref, state_ref, rates_ref, start_ref, fac_ref, mob_ref, *rest,
    halo, depth, first, with_rates, jacobi
):
    if with_rates:
        out_ref, out_rates_ref, goal_sc, *bufs = rest
    else:
        out_ref, goal_sc, *bufs = rest
        out_rates_ref = None
    node = sel_ref[pl.program_id(0)]
    count = rates_ref.shape[0]
    dt_tau = time_step * coef_ref[node, count]
    weights = [coef_ref[node, j] for j in range(count)]
    goal_planes = goal_sc.shape[1]
    off_goal = depth - (halo - 1)

    def goal_body(z, carry):
        acc = rates_ref[0, :, z] * weights[0]
        for j in range(1, count):
            acc = acc + rates_ref[j, :, z] * weights[j]
        goal_sc[:, z] = start_ref[:, z + off_goal] + time_step * acc - dt_tau * rates_ref[node, :, z]
        return carry

    lax.fori_loop(0, goal_planes, goal_body, 0)

    source = None
    for index in range(jacobi):
        target = out_ref if index + 1 == jacobi else bufs[index % len(bufs)]
        planes = goal_planes - 2 * index
        off_fac = depth - (halo - 1 - index)

        if index == 0 and first:
            def body(z, carry, target=target, off_fac=off_fac):
                f = fac_ref[0, :, z + off_fac]
                target_view = target.at[0] if target is out_ref else target
                target_view[:, z] = (goal_sc[:, z] + f * state_ref[:, z]) / (1.0 + 6.0 * f)
                return carry
        else:
            def body(z, carry, target=target, off_fac=off_fac, source=source, index=index):
                if source is None:
                    src = state_ref.at[0]
                else:
                    src = source
                f = fac_ref[0, :, z + off_fac]
                center = src[:, z + 1]
                near = plane_near(src[:, z], center, src[:, z + 2])
                value = (goal_sc[:, z + index] + f * (near - plane_drive(center))) / (1.0 + 6.0 * f)
                target_view = target.at[0] if target is out_ref else target
                target_view[:, z] = value
                return carry

        lax.fori_loop(0, planes, body, 0)
        source = target.at[0] if target is out_ref else target

    if with_rates:
        final_halo = halo - jacobi
        off_mob = depth - (final_halo - 1)

        def rate_body(z, carry):
            src = out_ref.at[0]
            mob = mob_ref[0, :, z + off_mob]
            center = src[:, z + 1]
            near = plane_near(src[:, z], center, src[:, z + 2])
            out_rates_ref[0, :, z] = -mob * (plane_drive(center) - (near - 6.0 * center))
            return carry

        lax.fori_loop(0, out_rates_ref.shape[2], rate_body, 0)


def sweep_call(sel, coef, state, rates, start, factor, mobility, halo, depth, first, with_rates):
    count, order, goal_planes, rows, lanes = rates.shape
    picks = sel.shape[0]
    out_planes = goal_planes - 2 * (JACOBI - 1)
    whole5 = lambda i, sel_ref: (0, 0, 0, 0, 0)
    whole4 = lambda i, sel_ref: (0, 0, 0, 0)
    per_node = lambda i, sel_ref: (sel_ref[i], 0, 0, 0, 0)
    per_out = lambda i, sel_ref: (i, 0, 0, 0, 0)
    if first:
        state_spec = pl.BlockSpec(state.shape, whole4)
    else:
        state_spec = pl.BlockSpec((1,) + state.shape[1:], per_node)
    in_specs = [
        pl.BlockSpec(memory_space=pltpu.SMEM),
        state_spec,
        pl.BlockSpec(rates.shape, whole5),
        pl.BlockSpec(start.shape, whole4),
        pl.BlockSpec((1,) + factor.shape[1:], per_node),
        pl.BlockSpec((1,) + mobility.shape[1:], per_node),
    ]
    out_shape = [jax.ShapeDtypeStruct((picks, order, out_planes, rows, lanes), jnp.float32)]
    out_specs = [pl.BlockSpec((1, order, out_planes, rows, lanes), per_out)]
    if with_rates:
        out_shape.append(jax.ShapeDtypeStruct((picks, order, out_planes - 2, rows, lanes), jnp.float32))
        out_specs.append(pl.BlockSpec((1, order, out_planes - 2, rows, lanes), per_out))
    scratch = [pltpu.VMEM((order, goal_planes, rows, lanes), jnp.float32)]
    scratch += [pltpu.VMEM((order, goal_planes, rows, lanes), jnp.float32) for _ in range(min(2, JACOBI - 1))]
    kernel = functools.partial(
        sweep_kernel, halo=halo, depth=depth, first=first, with_rates=with_rates, jacobi=JACOBI
    )
    result = pl.pallas_call(
        kernel,
        out_shape=tuple(out_shape),
        grid_spec=pltpu.PrefetchScalarGridSpec(
            num_scalar_prefetch=1,
            grid=(picks,),
            in_specs=in_specs,
            out_specs=tuple(out_specs),
            scratch_shapes=scratch,
        ),
        compiler_params=pltpu.CompilerParams(vmem_limit_bytes=60 * 1024 * 1024),
    )(sel, coef, state, rates, start, factor, mobility)
    return result


def on_device(grain_ids, peak_heat):
    total_nodes = lax.axis_size("node") * NODE_DEV
    node_times, table = radau_table(total_nodes)
    times = jnp.asarray(node_times, jnp.float32)
    taus = times.reshape((total_nodes, 1, 1, 1, 1))
    coef = jnp.asarray(
        np.concatenate([table, node_times[:, None]], axis=1).astype(np.float32)
    )
    mine = lax.axis_index("node") * NODE_DEV
    depth = SWEEPS * JACOBI
    orders = jnp.arange(P_SIZE, dtype=jnp.int32)
    every = jnp.arange(total_nodes, dtype=jnp.int32)

    packed = jnp.stack([grain_ids.astype(jnp.float32), peak_heat])
    packed = gather_halo(packed, 1, depth)
    ids_wide = packed[0]
    peak_wide = packed[1]
    start = (ids_wide[None] == orders[:, None, None, None].astype(jnp.float32)).astype(jnp.float32)

    states = None
    for step_index in range(STEPS):
        last_step = step_index + 1 == STEPS
        moments = (step_index + times) * time_step
        mobility = heat_mobility(peak_wide[None], moments[:, None, None, None])[:, None]
        factor = time_step * taus * mobility
        bracket, pull = prep_call(start)
        rates = -trim(mobility, 1) * bracket[None]
        halo = depth
        states = pull
        for sweep_index in range(SWEEPS):
            last = sweep_index + 1 == SWEEPS
            if last:
                keep = mine if last_step else total_nodes - 1
                sel = jnp.reshape(jnp.asarray(keep, jnp.int32), (1,))
            else:
                sel = every
            outs = sweep_call(
                sel, coef, states, rates, start, factor, mobility,
                halo, depth, sweep_index == 0, not last,
            )
            states = outs[0]
            if not last:
                rates = outs[1]
            halo -= JACOBI
        if not last_step:
            start = gather_halo(states[0], 1, depth)
    return states


def solution(mesh):
    in_specs = (P("space", None, None), P("space", None, None))
    out_specs = P("node", None, "space", None, None)
    return jax.shard_map(
        on_device, mesh=mesh, in_specs=in_specs, out_specs=out_specs, check_vma=False
    )
```

```python
import functools
import math

import jax
import jax.numpy as jnp
import numpy as np
from jax import lax
from jax.experimental import pallas as pl
from jax.experimental.pallas import tpu as pltpu
from jax.sharding import PartitionSpec as P

P_SIZE = 8
NODE_DEV = 1
SWEEPS = 3
JACOBI = 2
STEPS = 2


time_step = 0.25
cross_coef = 1.5
base_heat = 0.45
activation = 3.0


def gather_halo(block, dim, width):
    axis = "space"
    count = lax.axis_size(axis)
    size = block.shape[dim]
    lows = []
    highs = []
    distance = 1
    left = width
    while left > 0:
        take = min(size, left)
        up = [(i, (i + distance) % count) for i in range(count)]
        down = [(i, (i - distance) % count) for i in range(count)]
        lows.insert(0, lax.ppermute(lax.slice_in_dim(block, size - take, size, axis=dim), axis, up))
        highs.append(lax.ppermute(lax.slice_in_dim(block, 0, take, axis=dim), axis, down))
        left -= take
        distance += 1
    return jnp.concatenate(lows + [block] + highs, axis=dim)


def trim(block, count, dim=-3):
    if count == 0:
        return block
    return lax.slice_in_dim(block, count, block.shape[dim] - count, axis=dim)


def legendre_pair(count, point):
    before = 1.0
    current = point
    for degree in range(2, count + 1):
        following = ((2 * degree - 1) * point * current - (degree - 1) * before) / degree
        before = current
        current = following
    return (current, before)


def radau_value(count, point):
    high, low = legendre_pair(count, point)
    high_prev, low_prev = legendre_pair(count - 1, point)
    value = high - low
    slope_high = count * (point * high - low) / (point * point - 1.0)
    slope_low = (count - 1) * (point * high_prev - low_prev) / (point * point - 1.0)
    return (value, slope_high - slope_low)


def radau_table(count):
    roots = [1.0]
    for index in range(1, count):
        point = math.cos(2.0 * math.pi * index / (2 * count - 1))
        for repeat in range(100):
            value, slope = radau_value(count, point)
            point = point - value / slope
        roots.append(point)
    roots = sorted(roots)
    times_list = [(value + 1.0) / 2.0 for value in roots]
    times_list[-1] = 1.0
    table = []
    for row_index in range(count):
        upper = times_list[row_index]
        row_values = []
        for column in range(count):
            poly = [1.0]
            for other in range(count):
                if other != column:
                    scale = times_list[column] - times_list[other]
                    shifted = [0.0] + poly
                    scaled = [c * times_list[other] for c in poly] + [0.0]
                    poly = [(shifted[i] - scaled[i]) / scale for i in range(len(shifted))]
            integral_value = 0.0
            for power in range(len(poly)):
                integral_value += poly[power] * upper ** (power + 1) / (power + 1)
            row_values.append(integral_value)
        table.append(row_values)
    return (np.array(times_list), np.array(table))


def drive(field):
    squares = field * field
    total = jnp.sum(squares, axis=-4, keepdims=True)
    return -field + squares * field + 2.0 * cross_coef * field * (total - squares)


def near_sum(extended):
    inner = extended[..., 1:-1, :, :]
    result = extended[..., 2:, :, :] + extended[..., :-2, :, :]
    result = result + jnp.roll(inner, -1, -2) + jnp.roll(inner, 1, -2)
    return result + jnp.roll(inner, -1, -1) + jnp.roll(inner, 1, -1)


def heat_mobility(peak, moment):
    middle = 0.5 * time_step * STEPS
    theta = base_heat + (peak - base_heat) * jnp.exp(-(((moment - middle) / middle) ** 2))
    return jnp.exp(activation * (1.0 - 1.0 / theta))


def rate_on(extended, mobility):
    inner = extended[..., 1:-1, :, :]
    return -mobility * (drive(inner) - (near_sum(extended) - 6.0 * inner))


def relax_on(extended, goal, factor):
    inner = extended[..., 1:-1, :, :]
    return (goal + factor * (near_sum(extended) - drive(inner))) / (1.0 + 6.0 * factor)


def plane_near(below, center, above):
    result = above + below
    result = result + pltpu.roll(center, center.shape[1] - 1, 1) + pltpu.roll(center, 1, 1)
    return result + pltpu.roll(center, center.shape[2] - 1, 2) + pltpu.roll(center, 1, 2)


def plane_drive(field):
    squares = field * field
    total = jnp.sum(squares, axis=0, keepdims=True)
    return -field + squares * field + 2.0 * cross_coef * field * (total - squares)


def prep_kernel(start_ref, bracket_ref, pull_ref):
    def body(z, carry):
        center = start_ref[:, z + 1]
        near = plane_near(start_ref[:, z], center, start_ref[:, z + 2])
        push = plane_drive(center)
        bracket_ref[:, z] = push - (near - 6.0 * center)
        pull_ref[:, z] = near - push
        return carry

    lax.fori_loop(0, bracket_ref.shape[1], body, 0)


def prep_call(start):
    count, planes, rows, lanes = start.shape
    shape = jax.ShapeDtypeStruct((count, planes - 2, rows, lanes), jnp.float32)
    return pl.pallas_call(
        prep_kernel,
        out_shape=(shape, shape),
        in_specs=[pl.BlockSpec(memory_space=pltpu.VMEM)],
        out_specs=(pl.BlockSpec(memory_space=pltpu.VMEM), pl.BlockSpec(memory_space=pltpu.VMEM)),
    )(start)


def sweep_kernel(
    sel_ref, coef_ref, state_ref, rates_ref, start_ref, fac_ref, mob_ref, *rest,
    halo, depth, first, with_rates, jacobi
):
    if with_rates:
        out_ref, out_rates_ref, goal_sc, *bufs = rest
    else:
        out_ref, goal_sc, *bufs = rest
        out_rates_ref = None
    node = sel_ref[pl.program_id(0)]
    count = rates_ref.shape[0]
    if not first:
        dt_tau = time_step * coef_ref[node, count]
        weights = [coef_ref[node, j] for j in range(count)]
    if first:
        count = mob_ref.shape[0]
        weights = [coef_ref[node, j] for j in range(count)]
        dt_tau = time_step * coef_ref[node, count]
    goal_planes = goal_sc.shape[1]
    off_goal = depth - (halo - 1)

    def goal_body(z, carry):
        if first:
            bracket = rates_ref[:, z]
            mix = -mob_ref[0, :, z + off_goal] * weights[0]
            for j in range(1, count):
                mix = mix + -mob_ref[j, :, z + off_goal] * weights[j]
            own = -mob_ref[node, :, z + off_goal] * bracket
            goal_sc[:, z] = start_ref[:, z + off_goal] + time_step * (mix * bracket) - dt_tau * own
        else:
            acc = rates_ref[0, :, z] * weights[0]
            for j in range(1, count):
                acc = acc + rates_ref[j, :, z] * weights[j]
            goal_sc[:, z] = start_ref[:, z + off_goal] + time_step * acc - dt_tau * rates_ref[node, :, z]
        return carry

    lax.fori_loop(0, goal_planes, goal_body, 0)

    source = None
    for index in range(jacobi):
        target = out_ref if index + 1 == jacobi else bufs[index % len(bufs)]
        planes = goal_planes - 2 * index
        off_fac = depth - (halo - 1 - index)

        if index == 0 and first:
            def body(z, carry, target=target, off_fac=off_fac):
                f = fac_ref[0, :, z + off_fac]
                inv = 1.0 / (1.0 + 6.0 * f)
                target_view = target.at[0] if target is out_ref else target
                target_view[:, z] = (goal_sc[:, z] + f * state_ref[:, z]) * inv
                return carry
        else:
            def body(z, carry, target=target, off_fac=off_fac, source=source, index=index):
                if source is None:
                    src = state_ref.at[0]
                else:
                    src = source
                f = fac_ref[0, :, z + off_fac]
                center = src[:, z + 1]
                near = plane_near(src[:, z], center, src[:, z + 2])
                inv = 1.0 / (1.0 + 6.0 * f)
                value = (goal_sc[:, z + index] + f * (near - plane_drive(center))) * inv
                target_view = target.at[0] if target is out_ref else target
                target_view[:, z] = value
                return carry

        lax.fori_loop(0, planes, body, 0)
        source = target.at[0] if target is out_ref else target

    if with_rates:
        final_halo = halo - jacobi
        off_mob = depth - (final_halo - 1)

        def rate_body(z, carry):
            src = out_ref.at[0]
            mob = mob_ref[node if first else 0, :, z + off_mob]
            center = src[:, z + 1]
            near = plane_near(src[:, z], center, src[:, z + 2])
            out_rates_ref[0, :, z] = -mob * (plane_drive(center) - (near - 6.0 * center))
            return carry

        lax.fori_loop(0, out_rates_ref.shape[2], rate_body, 0)


def sweep_call(sel, coef, state, rates, start, factor, mobility, halo, depth, first, with_rates):
    order, goal_planes, rows, lanes = rates.shape[-4:]
    picks = sel.shape[0]
    out_planes = goal_planes - 2 * (JACOBI - 1)
    whole5 = lambda i, sel_ref: (0, 0, 0, 0, 0)
    whole4 = lambda i, sel_ref: (0, 0, 0, 0)
    per_node = lambda i, sel_ref: (sel_ref[i], 0, 0, 0, 0)
    per_out = lambda i, sel_ref: (i, 0, 0, 0, 0)
    if first:
        state_spec = pl.BlockSpec(state.shape, whole4)
    else:
        state_spec = pl.BlockSpec((1,) + state.shape[1:], per_node)
    in_specs = [
        pl.BlockSpec(memory_space=pltpu.SMEM),
        state_spec,
        pl.BlockSpec(rates.shape, whole4 if first else whole5),
        pl.BlockSpec(start.shape, whole4),
        pl.BlockSpec((1,) + factor.shape[1:], per_node),
        pl.BlockSpec(mobility.shape, whole5) if first else pl.BlockSpec((1,) + mobility.shape[1:], per_node),
    ]
    out_shape = [jax.ShapeDtypeStruct((picks, order, out_planes, rows, lanes), jnp.float32)]
    out_specs = [pl.BlockSpec((1, order, out_planes, rows, lanes), per_out)]
    if with_rates:
        out_shape.append(jax.ShapeDtypeStruct((picks, order, out_planes - 2, rows, lanes), jnp.float32))
        out_specs.append(pl.BlockSpec((1, order, out_planes - 2, rows, lanes), per_out))
    scratch = [pltpu.VMEM((order, goal_planes, rows, lanes), jnp.float32)]
    scratch += [pltpu.VMEM((order, goal_planes, rows, lanes), jnp.float32) for _ in range(min(2, JACOBI - 1))]
    kernel = functools.partial(
        sweep_kernel, halo=halo, depth=depth, first=first, with_rates=with_rates, jacobi=JACOBI
    )
    result = pl.pallas_call(
        kernel,
        out_shape=tuple(out_shape),
        grid_spec=pltpu.PrefetchScalarGridSpec(
            num_scalar_prefetch=1,
            grid=(picks,),
            in_specs=in_specs,
            out_specs=tuple(out_specs),
            scratch_shapes=scratch,
        ),
        compiler_params=pltpu.CompilerParams(vmem_limit_bytes=60 * 1024 * 1024),
    )(sel, coef, state, rates, start, factor, mobility)
    return result


def on_device(grain_ids, peak_heat):
    total_nodes = lax.axis_size("node") * NODE_DEV
    node_times, table = radau_table(total_nodes)
    times = jnp.asarray(node_times, jnp.float32)
    taus = times.reshape((total_nodes, 1, 1, 1, 1))
    coef = jnp.asarray(
        np.concatenate([table, node_times[:, None]], axis=1).astype(np.float32)
    )
    mine = lax.axis_index("node") * NODE_DEV
    depth = SWEEPS * JACOBI
    orders = jnp.arange(P_SIZE, dtype=jnp.int32)
    every = jnp.arange(total_nodes, dtype=jnp.int32)

    packed = jnp.stack([grain_ids.astype(jnp.float32), peak_heat])
    packed = gather_halo(packed, 1, depth)
    ids_wide = packed[0]
    peak_wide = packed[1]
    start = (ids_wide[None] == orders[:, None, None, None].astype(jnp.float32)).astype(jnp.float32)

    states = None
    for step_index in range(STEPS):
        last_step = step_index + 1 == STEPS
        moments = (step_index + times) * time_step
        mobility = heat_mobility(peak_wide[None], moments[:, None, None, None])[:, None]
        factor = time_step * taus * mobility
        rates, pull = prep_call(start)
        halo = depth
        states = pull
        for sweep_index in range(SWEEPS):
            last = sweep_index + 1 == SWEEPS
            if last:
                keep = mine if last_step else total_nodes - 1
                sel = jnp.reshape(jnp.asarray(keep, jnp.int32), (1,))
            else:
                sel = every
            outs = sweep_call(
                sel, coef, states, rates, start, factor, mobility,
                halo, depth, sweep_index == 0, not last,
            )
            states = outs[0]
            if not last:
                rates = outs[1]
            halo -= JACOBI
        if not last_step:
            start = gather_halo(states[0], 1, depth)
    return states


def solution(mesh):
    in_specs = (P("space", None, None), P("space", None, None))
    out_specs = P("node", None, "space", None, None)
    return jax.shard_map(
        on_device, mesh=mesh, in_specs=in_specs, out_specs=out_specs, check_vma=False
    )
```

```python
import functools
import math

import jax
import jax.numpy as jnp
import numpy as np
from jax import lax
from jax.experimental import pallas as pl
from jax.experimental.pallas import tpu as pltpu
from jax.sharding import PartitionSpec as P

P_SIZE = 8
NODE_DEV = 1
SWEEPS = 3
JACOBI = 2
STEPS = 2


time_step = 0.25
cross_coef = 1.5
base_heat = 0.45
activation = 3.0


def gather_halo(block, dim, width):
    axis = "space"
    count = lax.axis_size(axis)
    size = block.shape[dim]
    lows = []
    highs = []
    distance = 1
    left = width
    while left > 0:
        take = min(size, left)
        up = [(i, (i + distance) % count) for i in range(count)]
        down = [(i, (i - distance) % count) for i in range(count)]
        lows.insert(0, lax.ppermute(lax.slice_in_dim(block, size - take, size, axis=dim), axis, up))
        highs.append(lax.ppermute(lax.slice_in_dim(block, 0, take, axis=dim), axis, down))
        left -= take
        distance += 1
    return jnp.concatenate(lows + [block] + highs, axis=dim)


def trim(block, count, dim=-3):
    if count == 0:
        return block
    return lax.slice_in_dim(block, count, block.shape[dim] - count, axis=dim)


def legendre_pair(count, point):
    before = 1.0
    current = point
    for degree in range(2, count + 1):
        following = ((2 * degree - 1) * point * current - (degree - 1) * before) / degree
        before = current
        current = following
    return (current, before)


def radau_value(count, point):
    high, low = legendre_pair(count, point)
    high_prev, low_prev = legendre_pair(count - 1, point)
    value = high - low
    slope_high = count * (point * high - low) / (point * point - 1.0)
    slope_low = (count - 1) * (point * high_prev - low_prev) / (point * point - 1.0)
    return (value, slope_high - slope_low)


def radau_table(count):
    roots = [1.0]
    for index in range(1, count):
        point = math.cos(2.0 * math.pi * index / (2 * count - 1))
        for repeat in range(100):
            value, slope = radau_value(count, point)
            point = point - value / slope
        roots.append(point)
    roots = sorted(roots)
    times_list = [(value + 1.0) / 2.0 for value in roots]
    times_list[-1] = 1.0
    table = []
    for row_index in range(count):
        upper = times_list[row_index]
        row_values = []
        for column in range(count):
            poly = [1.0]
            for other in range(count):
                if other != column:
                    scale = times_list[column] - times_list[other]
                    shifted = [0.0] + poly
                    scaled = [c * times_list[other] for c in poly] + [0.0]
                    poly = [(shifted[i] - scaled[i]) / scale for i in range(len(shifted))]
            integral_value = 0.0
            for power in range(len(poly)):
                integral_value += poly[power] * upper ** (power + 1) / (power + 1)
            row_values.append(integral_value)
        table.append(row_values)
    return (np.array(times_list), np.array(table))


def drive(field):
    squares = field * field
    total = jnp.sum(squares, axis=-4, keepdims=True)
    return -field + squares * field + 2.0 * cross_coef * field * (total - squares)


def near_sum(extended):
    inner = extended[..., 1:-1, :, :]
    result = extended[..., 2:, :, :] + extended[..., :-2, :, :]
    result = result + jnp.roll(inner, -1, -2) + jnp.roll(inner, 1, -2)
    return result + jnp.roll(inner, -1, -1) + jnp.roll(inner, 1, -1)


def heat_mobility(peak, moment):
    middle = 0.5 * time_step * STEPS
    theta = base_heat + (peak - base_heat) * jnp.exp(-(((moment - middle) / middle) ** 2))
    return jnp.exp(activation * (1.0 - 1.0 / theta))


def rate_on(extended, mobility):
    inner = extended[..., 1:-1, :, :]
    return -mobility * (drive(inner) - (near_sum(extended) - 6.0 * inner))


def relax_on(extended, goal, factor):
    inner = extended[..., 1:-1, :, :]
    return (goal + factor * (near_sum(extended) - drive(inner))) / (1.0 + 6.0 * factor)


def plane_near(below, center, above):
    result = above + below
    result = result + pltpu.roll(center, center.shape[1] - 1, 1) + pltpu.roll(center, 1, 1)
    return result + pltpu.roll(center, center.shape[2] - 1, 2) + pltpu.roll(center, 1, 2)


def plane_drive(field):
    squares = field * field
    total = jnp.sum(squares, axis=0, keepdims=True)
    return field * ((2.0 * cross_coef * total - 1.0) - (2.0 * cross_coef - 1.0) * squares)


def prep_kernel(start_ref, bracket_ref, pull_ref):
    def body(z, carry):
        center = start_ref[:, z + 1]
        near = plane_near(start_ref[:, z], center, start_ref[:, z + 2])
        push = plane_drive(center)
        bracket_ref[:, z] = push - (near - 6.0 * center)
        pull_ref[:, z] = near - push
        return carry

    lax.fori_loop(0, bracket_ref.shape[1], body, 0, unroll=True)


def prep_call(start):
    count, planes, rows, lanes = start.shape
    shape = jax.ShapeDtypeStruct((count, planes - 2, rows, lanes), jnp.float32)
    return pl.pallas_call(
        prep_kernel,
        out_shape=(shape, shape),
        in_specs=[pl.BlockSpec(memory_space=pltpu.VMEM)],
        out_specs=(pl.BlockSpec(memory_space=pltpu.VMEM), pl.BlockSpec(memory_space=pltpu.VMEM)),
    )(start)


def sweep_kernel(
    sel_ref, coef_ref, state_ref, rates_ref, start_ref, fac_ref, mob_ref, *rest,
    halo, depth, first, with_rates, jacobi
):
    if with_rates:
        out_ref, out_rates_ref, goal_sc, *bufs = rest
    else:
        out_ref, goal_sc, *bufs = rest
        out_rates_ref = None
    node = sel_ref[pl.program_id(0)]
    count = rates_ref.shape[0]
    if not first:
        dt_tau = time_step * coef_ref[node, count]
        weights = [coef_ref[node, j] for j in range(count)]
    if first:
        count = mob_ref.shape[0]
        weights = [coef_ref[node, j] for j in range(count)]
        dt_tau = time_step * coef_ref[node, count]
    goal_planes = goal_sc.shape[1]
    off_goal = depth - (halo - 1)

    def goal_body(z, carry):
        if first:
            bracket = rates_ref[:, z]
            mix = -mob_ref[0, :, z + off_goal] * weights[0]
            for j in range(1, count):
                mix = mix + -mob_ref[j, :, z + off_goal] * weights[j]
            own = -mob_ref[node, :, z + off_goal] * bracket
            goal_sc[:, z] = start_ref[:, z + off_goal] + time_step * (mix * bracket) - dt_tau * own
        else:
            acc = rates_ref[0, :, z] * weights[0]
            for j in range(1, count):
                acc = acc + rates_ref[j, :, z] * weights[j]
            goal_sc[:, z] = start_ref[:, z + off_goal] + time_step * acc - dt_tau * rates_ref[node, :, z]
        return carry

    lax.fori_loop(0, goal_planes, goal_body, 0, unroll=True)

    source = None
    for index in range(jacobi):
        target = out_ref if index + 1 == jacobi else bufs[index % len(bufs)]
        planes = goal_planes - 2 * index
        off_fac = depth - (halo - 1 - index)

        if index == 0 and first:
            def body(z, carry, target=target, off_fac=off_fac):
                f = fac_ref[0, :, z + off_fac]
                inv = 1.0 / (1.0 + 6.0 * f)
                target_view = target.at[0] if target is out_ref else target
                target_view[:, z] = (goal_sc[:, z] + f * state_ref[:, z]) * inv
                return carry
        else:
            def body(z, carry, target=target, off_fac=off_fac, source=source, index=index):
                if source is None:
                    src = state_ref.at[0]
                else:
                    src = source
                f = fac_ref[0, :, z + off_fac]
                center = src[:, z + 1]
                near = plane_near(src[:, z], center, src[:, z + 2])
                inv = 1.0 / (1.0 + 6.0 * f)
                value = (goal_sc[:, z + index] + f * (near - plane_drive(center))) * inv
                target_view = target.at[0] if target is out_ref else target
                target_view[:, z] = value
                return carry

        lax.fori_loop(0, planes, body, 0, unroll=True)
        source = target.at[0] if target is out_ref else target

    if with_rates:
        final_halo = halo - jacobi
        off_mob = depth - (final_halo - 1)

        def rate_body(z, carry):
            src = out_ref.at[0]
            mob = mob_ref[node if first else 0, :, z + off_mob]
            center = src[:, z + 1]
            near = plane_near(src[:, z], center, src[:, z + 2])
            out_rates_ref[0, :, z] = -mob * (plane_drive(center) - (near - 6.0 * center))
            return carry

        lax.fori_loop(0, out_rates_ref.shape[2], rate_body, 0, unroll=True)


def sweep_call(sel, coef, state, rates, start, factor, mobility, halo, depth, first, with_rates):
    order, goal_planes, rows, lanes = rates.shape[-4:]
    picks = sel.shape[0]
    out_planes = goal_planes - 2 * (JACOBI - 1)
    whole5 = lambda i, sel_ref: (0, 0, 0, 0, 0)
    whole4 = lambda i, sel_ref: (0, 0, 0, 0)
    per_node = lambda i, sel_ref: (sel_ref[i], 0, 0, 0, 0)
    per_out = lambda i, sel_ref: (i, 0, 0, 0, 0)
    if first:
        state_spec = pl.BlockSpec(state.shape, whole4)
    else:
        state_spec = pl.BlockSpec((1,) + state.shape[1:], per_node)
    in_specs = [
        pl.BlockSpec(memory_space=pltpu.SMEM),
        state_spec,
        pl.BlockSpec(rates.shape, whole4 if first else whole5),
        pl.BlockSpec(start.shape, whole4),
        pl.BlockSpec((1,) + factor.shape[1:], per_node),
        pl.BlockSpec(mobility.shape, whole5) if first else pl.BlockSpec((1,) + mobility.shape[1:], per_node),
    ]
    out_shape = [jax.ShapeDtypeStruct((picks, order, out_planes, rows, lanes), jnp.float32)]
    out_specs = [pl.BlockSpec((1, order, out_planes, rows, lanes), per_out)]
    if with_rates:
        out_shape.append(jax.ShapeDtypeStruct((picks, order, out_planes - 2, rows, lanes), jnp.float32))
        out_specs.append(pl.BlockSpec((1, order, out_planes - 2, rows, lanes), per_out))
    scratch = [pltpu.VMEM((order, goal_planes, rows, lanes), jnp.float32)]
    scratch += [pltpu.VMEM((order, goal_planes, rows, lanes), jnp.float32) for _ in range(min(2, JACOBI - 1))]
    kernel = functools.partial(
        sweep_kernel, halo=halo, depth=depth, first=first, with_rates=with_rates, jacobi=JACOBI
    )
    result = pl.pallas_call(
        kernel,
        out_shape=tuple(out_shape),
        grid_spec=pltpu.PrefetchScalarGridSpec(
            num_scalar_prefetch=1,
            grid=(picks,),
            in_specs=in_specs,
            out_specs=tuple(out_specs),
            scratch_shapes=scratch,
        ),
        compiler_params=pltpu.CompilerParams(vmem_limit_bytes=60 * 1024 * 1024),
    )(sel, coef, state, rates, start, factor, mobility)
    return result


def on_device(grain_ids, peak_heat):
    total_nodes = lax.axis_size("node") * NODE_DEV
    node_times, table = radau_table(total_nodes)
    times = jnp.asarray(node_times, jnp.float32)
    taus = times.reshape((total_nodes, 1, 1, 1, 1))
    coef = jnp.asarray(
        np.concatenate([table, node_times[:, None]], axis=1).astype(np.float32)
    )
    mine = lax.axis_index("node") * NODE_DEV
    depth = SWEEPS * JACOBI
    orders = jnp.arange(P_SIZE, dtype=jnp.int32)
    every = jnp.arange(total_nodes, dtype=jnp.int32)

    packed = jnp.stack([grain_ids.astype(jnp.float32), peak_heat])
    packed = gather_halo(packed, 1, depth)
    ids_wide = packed[0]
    peak_wide = packed[1]
    start = (ids_wide[None] == orders[:, None, None, None].astype(jnp.float32)).astype(jnp.float32)

    states = None
    for step_index in range(STEPS):
        last_step = step_index + 1 == STEPS
        moments = (step_index + times) * time_step
        mobility = heat_mobility(peak_wide[None], moments[:, None, None, None])[:, None]
        factor = time_step * taus * mobility
        rates, pull = prep_call(start)
        halo = depth
        states = pull
        for sweep_index in range(SWEEPS):
            last = sweep_index + 1 == SWEEPS
            if last:
                keep = mine if last_step else total_nodes - 1
                sel = jnp.reshape(jnp.asarray(keep, jnp.int32), (1,))
            else:
                sel = every
            outs = sweep_call(
                sel, coef, states, rates, start, factor, mobility,
                halo, depth, sweep_index == 0, not last,
            )
            states = outs[0]
            if not last:
                rates = outs[1]
            halo -= JACOBI
        if not last_step:
            start = gather_halo(states[0], 1, depth)
    return states


def solution(mesh):
    in_specs = (P("space", None, None), P("space", None, None))
    out_specs = P("node", None, "space", None, None)
    return jax.shard_map(
        on_device, mesh=mesh, in_specs=in_specs, out_specs=out_specs, check_vma=False
    )
```

```python
import functools
import math

import jax
import jax.numpy as jnp
import numpy as np
from jax import lax
from jax.experimental import pallas as pl
from jax.experimental.pallas import tpu as pltpu
from jax.sharding import PartitionSpec as P

P_SIZE = 8
NODE_DEV = 1
SWEEPS = 3
JACOBI = 2
STEPS = 2


time_step = 0.25
cross_coef = 1.5
base_heat = 0.45
activation = 3.0


def gather_halo(block, dim, width):
    axis = "space"
    count = lax.axis_size(axis)
    size = block.shape[dim]
    lows = []
    highs = []
    distance = 1
    left = width
    while left > 0:
        take = min(size, left)
        up = [(i, (i + distance) % count) for i in range(count)]
        down = [(i, (i - distance) % count) for i in range(count)]
        lows.insert(0, lax.ppermute(lax.slice_in_dim(block, size - take, size, axis=dim), axis, up))
        highs.append(lax.ppermute(lax.slice_in_dim(block, 0, take, axis=dim), axis, down))
        left -= take
        distance += 1
    return jnp.concatenate(lows + [block] + highs, axis=dim)


def trim(block, count, dim=-3):
    if count == 0:
        return block
    return lax.slice_in_dim(block, count, block.shape[dim] - count, axis=dim)


def legendre_pair(count, point):
    before = 1.0
    current = point
    for degree in range(2, count + 1):
        following = ((2 * degree - 1) * point * current - (degree - 1) * before) / degree
        before = current
        current = following
    return (current, before)


def radau_value(count, point):
    high, low = legendre_pair(count, point)
    high_prev, low_prev = legendre_pair(count - 1, point)
    value = high - low
    slope_high = count * (point * high - low) / (point * point - 1.0)
    slope_low = (count - 1) * (point * high_prev - low_prev) / (point * point - 1.0)
    return (value, slope_high - slope_low)


def radau_table(count):
    roots = [1.0]
    for index in range(1, count):
        point = math.cos(2.0 * math.pi * index / (2 * count - 1))
        for repeat in range(100):
            value, slope = radau_value(count, point)
            point = point - value / slope
        roots.append(point)
    roots = sorted(roots)
    times_list = [(value + 1.0) / 2.0 for value in roots]
    times_list[-1] = 1.0
    table = []
    for row_index in range(count):
        upper = times_list[row_index]
        row_values = []
        for column in range(count):
            poly = [1.0]
            for other in range(count):
                if other != column:
                    scale = times_list[column] - times_list[other]
                    shifted = [0.0] + poly
                    scaled = [c * times_list[other] for c in poly] + [0.0]
                    poly = [(shifted[i] - scaled[i]) / scale for i in range(len(shifted))]
            integral_value = 0.0
            for power in range(len(poly)):
                integral_value += poly[power] * upper ** (power + 1) / (power + 1)
            row_values.append(integral_value)
        table.append(row_values)
    return (np.array(times_list), np.array(table))


def drive(field):
    squares = field * field
    total = jnp.sum(squares, axis=-4, keepdims=True)
    return -field + squares * field + 2.0 * cross_coef * field * (total - squares)


def near_sum(extended):
    inner = extended[..., 1:-1, :, :]
    result = extended[..., 2:, :, :] + extended[..., :-2, :, :]
    result = result + jnp.roll(inner, -1, -2) + jnp.roll(inner, 1, -2)
    return result + jnp.roll(inner, -1, -1) + jnp.roll(inner, 1, -1)


def heat_mobility(peak, moment):
    middle = 0.5 * time_step * STEPS
    theta = base_heat + (peak - base_heat) * jnp.exp(-(((moment - middle) / middle) ** 2))
    return jnp.exp(activation * (1.0 - 1.0 / theta))


def rate_on(extended, mobility):
    inner = extended[..., 1:-1, :, :]
    return -mobility * (drive(inner) - (near_sum(extended) - 6.0 * inner))


def relax_on(extended, goal, factor):
    inner = extended[..., 1:-1, :, :]
    return (goal + factor * (near_sum(extended) - drive(inner))) / (1.0 + 6.0 * factor)


def plane_near(below, center, above):
    even = center[:, 0:1]
    odd = center[:, 1:2]
    rows = center.shape[2]
    y_next = jnp.concatenate([odd, pltpu.roll(even, rows - 1, 2)], axis=1)
    y_prev = jnp.concatenate([pltpu.roll(odd, 1, 2), even], axis=1)
    result = above + below
    result = result + y_next + y_prev
    return result + pltpu.roll(center, center.shape[3] - 1, 3) + pltpu.roll(center, 1, 3)


def plane_drive(field):
    squares = field * field
    total = jnp.sum(squares, axis=0, keepdims=True)
    return field * ((2.0 * cross_coef * total - 1.0) - (2.0 * cross_coef - 1.0) * squares)


def prep_kernel(start_ref, bracket_ref, pull_ref):
    def body(z, carry):
        center = start_ref[:, z + 1]
        near = plane_near(start_ref[:, z], center, start_ref[:, z + 2])
        push = plane_drive(center)
        bracket_ref[:, z] = push - (near - 6.0 * center)
        pull_ref[:, z] = near - push
        return carry

    lax.fori_loop(0, bracket_ref.shape[1], body, 0, unroll=True)


def prep_call(start):
    count, planes = start.shape[:2]
    shape = jax.ShapeDtypeStruct((count, planes - 2) + start.shape[2:], jnp.float32)
    return pl.pallas_call(
        prep_kernel,
        out_shape=(shape, shape),
        in_specs=[pl.BlockSpec(memory_space=pltpu.VMEM)],
        out_specs=(pl.BlockSpec(memory_space=pltpu.VMEM), pl.BlockSpec(memory_space=pltpu.VMEM)),
    )(start)


def sweep_kernel(
    sel_ref, coef_ref, state_ref, rates_ref, start_ref, fac_ref, mob_ref, *rest,
    halo, depth, first, with_rates, jacobi
):
    if with_rates:
        out_ref, out_rates_ref, goal_sc, *bufs = rest
    else:
        out_ref, goal_sc, *bufs = rest
        out_rates_ref = None
    node = sel_ref[pl.program_id(0)]
    count = rates_ref.shape[0]
    if not first:
        dt_tau = time_step * coef_ref[node, count]
        weights = [coef_ref[node, j] for j in range(count)]
    if first:
        count = mob_ref.shape[0]
        weights = [coef_ref[node, j] for j in range(count)]
        dt_tau = time_step * coef_ref[node, count]
    goal_planes = goal_sc.shape[1]
    off_goal = depth - (halo - 1)

    def goal_body(z, carry):
        if first:
            bracket = rates_ref[:, z]
            mix = -mob_ref[0, :, z + off_goal] * weights[0]
            for j in range(1, count):
                mix = mix + -mob_ref[j, :, z + off_goal] * weights[j]
            own = -mob_ref[node, :, z + off_goal] * bracket
            goal_sc[:, z] = start_ref[:, z + off_goal] + time_step * (mix * bracket) - dt_tau * own
        else:
            acc = rates_ref[0, :, z] * weights[0]
            for j in range(1, count):
                acc = acc + rates_ref[j, :, z] * weights[j]
            goal_sc[:, z] = start_ref[:, z + off_goal] + time_step * acc - dt_tau * rates_ref[node, :, z]
        return carry

    lax.fori_loop(0, goal_planes, goal_body, 0, unroll=True)

    source = None
    for index in range(jacobi):
        target = out_ref if index + 1 == jacobi else bufs[index % len(bufs)]
        planes = goal_planes - 2 * index
        off_fac = depth - (halo - 1 - index)

        if index == 0 and first:
            def body(z, carry, target=target, off_fac=off_fac):
                f = fac_ref[0, :, z + off_fac]
                inv = 1.0 / (1.0 + 6.0 * f)
                target_view = target.at[0] if target is out_ref else target
                target_view[:, z] = (goal_sc[:, z] + f * state_ref[:, z]) * inv
                return carry
        else:
            def body(z, carry, target=target, off_fac=off_fac, source=source, index=index):
                if source is None:
                    src = state_ref.at[0]
                else:
                    src = source
                f = fac_ref[0, :, z + off_fac]
                center = src[:, z + 1]
                near = plane_near(src[:, z], center, src[:, z + 2])
                inv = 1.0 / (1.0 + 6.0 * f)
                value = (goal_sc[:, z + index] + f * (near - plane_drive(center))) * inv
                target_view = target.at[0] if target is out_ref else target
                target_view[:, z] = value
                return carry

        lax.fori_loop(0, planes, body, 0, unroll=True)
        source = target.at[0] if target is out_ref else target

    if with_rates:
        final_halo = halo - jacobi
        off_mob = depth - (final_halo - 1)

        def rate_body(z, carry):
            src = out_ref.at[0]
            mob = mob_ref[node if first else 0, :, z + off_mob]
            center = src[:, z + 1]
            near = plane_near(src[:, z], center, src[:, z + 2])
            out_rates_ref[0, :, z] = -mob * (plane_drive(center) - (near - 6.0 * center))
            return carry

        lax.fori_loop(0, out_rates_ref.shape[2], rate_body, 0, unroll=True)


def sweep_call(sel, coef, state, rates, start, factor, mobility, halo, depth, first, with_rates):
    order, goal_planes = start.shape[0], rates.shape[-4]
    plane = start.shape[2:]
    picks = sel.shape[0]
    out_planes = goal_planes - 2 * (JACOBI - 1)

    def whole(block):
        return pl.BlockSpec(block.shape, lambda i, sel_ref: (0,) * block.ndim)

    def per_node(block):
        return pl.BlockSpec(
            (1,) + block.shape[1:], lambda i, sel_ref: (sel_ref[i],) + (0,) * (block.ndim - 1)
        )

    def per_out(shape):
        return pl.BlockSpec((1,) + shape[1:], lambda i, sel_ref: (i,) + (0,) * (len(shape) - 1))

    in_specs = [
        pl.BlockSpec(memory_space=pltpu.SMEM),
        whole(state) if first else per_node(state),
        whole(rates),
        whole(start),
        per_node(factor),
        whole(mobility) if first else per_node(mobility),
    ]
    out_dims = [(picks, order, out_planes) + plane]
    if with_rates:
        out_dims.append((picks, order, out_planes - 2) + plane)
    out_shape = [jax.ShapeDtypeStruct(dims, jnp.float32) for dims in out_dims]
    out_specs = [per_out(dims) for dims in out_dims]
    scratch = [pltpu.VMEM((order, goal_planes) + plane, jnp.float32)]
    scratch += [pltpu.VMEM((order, goal_planes) + plane, jnp.float32) for _ in range(min(2, JACOBI - 1))]
    kernel = functools.partial(
        sweep_kernel, halo=halo, depth=depth, first=first, with_rates=with_rates, jacobi=JACOBI
    )
    result = pl.pallas_call(
        kernel,
        out_shape=tuple(out_shape),
        grid_spec=pltpu.PrefetchScalarGridSpec(
            num_scalar_prefetch=1,
            grid=(picks,),
            in_specs=in_specs,
            out_specs=tuple(out_specs),
            scratch_shapes=scratch,
        ),
        compiler_params=pltpu.CompilerParams(vmem_limit_bytes=60 * 1024 * 1024),
    )(sel, coef, state, rates, start, factor, mobility)
    return result


def on_device(grain_ids, peak_heat):
    total_nodes = lax.axis_size("node") * NODE_DEV
    node_times, table = radau_table(total_nodes)
    times = jnp.asarray(node_times, jnp.float32)
    taus = times.reshape((total_nodes, 1, 1, 1, 1, 1))
    coef = jnp.asarray(
        np.concatenate([table, node_times[:, None]], axis=1).astype(np.float32)
    )
    mine = lax.axis_index("node") * NODE_DEV
    depth = SWEEPS * JACOBI
    orders = jnp.arange(P_SIZE, dtype=jnp.int32)
    every = jnp.asarray(np.arange(total_nodes, dtype=np.int32))

    packed = jnp.stack([grain_ids.astype(jnp.float32), peak_heat])
    planes, rows, lanes = grain_ids.shape
    packed = packed.reshape((2, planes, rows // 2, 2, lanes)).transpose((0, 1, 3, 2, 4))
    packed = gather_halo(packed, 1, depth)
    ids_wide = packed[0]
    peak_wide = packed[1]
    start = (ids_wide[None] == orders[:, None, None, None, None].astype(jnp.float32)).astype(jnp.float32)

    states = None
    for step_index in range(STEPS):
        last_step = step_index + 1 == STEPS
        moments = (step_index + times) * time_step
        mobility = heat_mobility(peak_wide[None], moments[:, None, None, None, None])[:, None]
        factor = time_step * taus * mobility
        rates, pull = prep_call(start)
        halo = depth
        states = pull
        for sweep_index in range(SWEEPS):
            last = sweep_index + 1 == SWEEPS
            if last:
                keep = mine if last_step else total_nodes - 1
                if last_step:
                    sel = jnp.reshape(jnp.asarray(keep, jnp.int32), (1,))
                else:
                    sel = jnp.asarray(np.array([keep], np.int32))
            else:
                sel = every
            outs = sweep_call(
                sel, coef, states, rates, start, factor, mobility,
                halo, depth, sweep_index == 0, not last,
            )
            states = outs[0]
            if not last:
                rates = outs[1]
            halo -= JACOBI
        if not last_step:
            start = gather_halo(states[0], 1, depth)
    count, order, planes = states.shape[:3]
    return states.transpose((0, 1, 2, 4, 3, 5)).reshape((count, order, planes, rows, lanes))


def solution(mesh):
    in_specs = (P("space", None, None), P("space", None, None))
    out_specs = P("node", None, "space", None, None)
    return jax.shard_map(
        on_device, mesh=mesh, in_specs=in_specs, out_specs=out_specs, check_vma=False
    )
```

```python
import functools
import math

import jax
import jax.numpy as jnp
import numpy as np
from jax import lax
from jax.experimental import pallas as pl
from jax.experimental.pallas import tpu as pltpu
from jax.sharding import PartitionSpec as P

P_SIZE = 8
NODE_DEV = 1
SWEEPS = 3
JACOBI = 2
STEPS = 2


time_step = 0.25
cross_coef = 1.5
base_heat = 0.45
activation = 3.0


def gather_halo(block, dim, width):
    axis = "space"
    count = lax.axis_size(axis)
    size = block.shape[dim]
    lows = []
    highs = []
    distance = 1
    left = width
    while left > 0:
        take = min(size, left)
        up = [(i, (i + distance) % count) for i in range(count)]
        down = [(i, (i - distance) % count) for i in range(count)]
        lows.insert(0, lax.ppermute(lax.slice_in_dim(block, size - take, size, axis=dim), axis, up))
        highs.append(lax.ppermute(lax.slice_in_dim(block, 0, take, axis=dim), axis, down))
        left -= take
        distance += 1
    return jnp.concatenate(lows + [block] + highs, axis=dim)


def trim(block, count, dim=-3):
    if count == 0:
        return block
    return lax.slice_in_dim(block, count, block.shape[dim] - count, axis=dim)


def legendre_pair(count, point):
    before = 1.0
    current = point
    for degree in range(2, count + 1):
        following = ((2 * degree - 1) * point * current - (degree - 1) * before) / degree
        before = current
        current = following
    return (current, before)


def radau_value(count, point):
    high, low = legendre_pair(count, point)
    high_prev, low_prev = legendre_pair(count - 1, point)
    value = high - low
    slope_high = count * (point * high - low) / (point * point - 1.0)
    slope_low = (count - 1) * (point * high_prev - low_prev) / (point * point - 1.0)
    return (value, slope_high - slope_low)


def radau_table(count):
    roots = [1.0]
    for index in range(1, count):
        point = math.cos(2.0 * math.pi * index / (2 * count - 1))
        for repeat in range(100):
            value, slope = radau_value(count, point)
            point = point - value / slope
        roots.append(point)
    roots = sorted(roots)
    times_list = [(value + 1.0) / 2.0 for value in roots]
    times_list[-1] = 1.0
    table = []
    for row_index in range(count):
        upper = times_list[row_index]
        row_values = []
        for column in range(count):
            poly = [1.0]
            for other in range(count):
                if other != column:
                    scale = times_list[column] - times_list[other]
                    shifted = [0.0] + poly
                    scaled = [c * times_list[other] for c in poly] + [0.0]
                    poly = [(shifted[i] - scaled[i]) / scale for i in range(len(shifted))]
            integral_value = 0.0
            for power in range(len(poly)):
                integral_value += poly[power] * upper ** (power + 1) / (power + 1)
            row_values.append(integral_value)
        table.append(row_values)
    return (np.array(times_list), np.array(table))


def drive(field):
    squares = field * field
    total = jnp.sum(squares, axis=-4, keepdims=True)
    return -field + squares * field + 2.0 * cross_coef * field * (total - squares)


def near_sum(extended):
    inner = extended[..., 1:-1, :, :]
    result = extended[..., 2:, :, :] + extended[..., :-2, :, :]
    result = result + jnp.roll(inner, -1, -2) + jnp.roll(inner, 1, -2)
    return result + jnp.roll(inner, -1, -1) + jnp.roll(inner, 1, -1)


def heat_mobility(peak, moment):
    middle = 0.5 * time_step * STEPS
    theta = base_heat + (peak - base_heat) * jnp.exp(-(((moment - middle) / middle) ** 2))
    return jnp.exp(activation * (1.0 - 1.0 / theta))


def rate_on(extended, mobility):
    inner = extended[..., 1:-1, :, :]
    return -mobility * (drive(inner) - (near_sum(extended) - 6.0 * inner))


def relax_on(extended, goal, factor):
    inner = extended[..., 1:-1, :, :]
    return (goal + factor * (near_sum(extended) - drive(inner))) / (1.0 + 6.0 * factor)


def plane_near(below, center, above):
    even = center[:, 0:1]
    odd = center[:, 1:2]
    rows = center.shape[2]
    y_next = jnp.concatenate([odd, pltpu.roll(even, rows - 1, 2)], axis=1)
    y_prev = jnp.concatenate([pltpu.roll(odd, 1, 2), even], axis=1)
    result = above + below
    result = result + y_next + y_prev
    return result + pltpu.roll(center, center.shape[3] - 1, 3) + pltpu.roll(center, 1, 3)


def plane_drive(field):
    squares = field * field
    total = jnp.sum(squares, axis=0, keepdims=True)
    return field * ((2.0 * cross_coef * total - 1.0) - (2.0 * cross_coef - 1.0) * squares)


def prep_kernel(start_ref, bracket_ref, pull_ref):
    def body(z, carry):
        center = start_ref[:, z + 1]
        near = plane_near(start_ref[:, z], center, start_ref[:, z + 2])
        push = plane_drive(center)
        bracket_ref[:, z] = push - (near - 6.0 * center)
        pull_ref[:, z] = near - push
        return carry

    lax.fori_loop(0, bracket_ref.shape[1], body, 0, unroll=True)


def prep_call(start):
    count, planes = start.shape[:2]
    shape = jax.ShapeDtypeStruct((count, planes - 2) + start.shape[2:], jnp.float32)
    return pl.pallas_call(
        prep_kernel,
        out_shape=(shape, shape),
        in_specs=[pl.BlockSpec(memory_space=pltpu.VMEM)],
        out_specs=(pl.BlockSpec(memory_space=pltpu.VMEM), pl.BlockSpec(memory_space=pltpu.VMEM)),
    )(start)


def sweep_kernel(
    sel_ref, coef_ref, state_ref, rates_ref, start_ref, fac_ref, mob_ref, *rest,
    halo, depth, first, with_rates, jacobi
):
    if with_rates:
        out_ref, out_rates_ref, goal_sc, *bufs = rest
    else:
        out_ref, goal_sc, *bufs = rest
        out_rates_ref = None
    node = sel_ref[pl.program_id(0)]
    count = rates_ref.shape[0]
    if first:
        count = mob_ref.shape[0]
    weights = [coef_ref[node, j] for j in range(count)]
    goal_planes = goal_sc.shape[1]
    off_goal = depth - (halo - 1)

    def goal_body(z, carry):
        if first:
            bracket = rates_ref[:, z]
            mix = -mob_ref[0, :, z + off_goal] * weights[0]
            for j in range(1, count):
                mix = mix + -mob_ref[j, :, z + off_goal] * weights[j]
            goal_sc[:, z] = start_ref[:, z + off_goal] + mix * bracket
        else:
            acc = rates_ref[0, :, z] * weights[0]
            for j in range(1, count):
                acc = acc + rates_ref[j, :, z] * weights[j]
            goal_sc[:, z] = start_ref[:, z + off_goal] + acc
        return carry

    lax.fori_loop(0, goal_planes, goal_body, 0, unroll=True)

    source = None
    for index in range(jacobi):
        target = out_ref if index + 1 == jacobi else bufs[index % len(bufs)]
        planes = goal_planes - 2 * index
        off_fac = depth - (halo - 1 - index)

        if index == 0 and first:
            def body(z, carry, target=target, off_fac=off_fac):
                f = fac_ref[0, :, z + off_fac]
                inv = 1.0 / (1.0 + 6.0 * f)
                target_view = target.at[0] if target is out_ref else target
                target_view[:, z] = (goal_sc[:, z] + f * state_ref[:, z]) * inv
                return carry
        else:
            def body(z, carry, target=target, off_fac=off_fac, source=source, index=index):
                if source is None:
                    src = state_ref.at[0]
                else:
                    src = source
                f = fac_ref[0, :, z + off_fac]
                center = src[:, z + 1]
                near = plane_near(src[:, z], center, src[:, z + 2])
                inv = 1.0 / (1.0 + 6.0 * f)
                value = (goal_sc[:, z + index] + f * (near - plane_drive(center))) * inv
                target_view = target.at[0] if target is out_ref else target
                target_view[:, z] = value
                return carry

        lax.fori_loop(0, planes, body, 0, unroll=True)
        source = target.at[0] if target is out_ref else target

    if with_rates:
        final_halo = halo - jacobi
        off_mob = depth - (final_halo - 1)

        def rate_body(z, carry):
            src = out_ref.at[0]
            mob = mob_ref[node if first else 0, :, z + off_mob]
            center = src[:, z + 1]
            near = plane_near(src[:, z], center, src[:, z + 2])
            out_rates_ref[0, :, z] = -mob * (plane_drive(center) - (near - 6.0 * center))
            return carry

        lax.fori_loop(0, out_rates_ref.shape[2], rate_body, 0, unroll=True)


def sweep_call(sel, coef, state, rates, start, factor, mobility, halo, depth, first, with_rates):
    order, goal_planes = start.shape[0], rates.shape[-4]
    plane = start.shape[2:]
    picks = sel.shape[0]
    out_planes = goal_planes - 2 * (JACOBI - 1)

    def whole(block):
        return pl.BlockSpec(block.shape, lambda i, sel_ref: (0,) * block.ndim)

    def per_node(block):
        return pl.BlockSpec(
            (1,) + block.shape[1:], lambda i, sel_ref: (sel_ref[i],) + (0,) * (block.ndim - 1)
        )

    def per_out(shape):
        return pl.BlockSpec((1,) + shape[1:], lambda i, sel_ref: (i,) + (0,) * (len(shape) - 1))

    in_specs = [
        pl.BlockSpec(memory_space=pltpu.SMEM),
        whole(state) if first else per_node(state),
        whole(rates),
        whole(start),
        per_node(factor),
        whole(mobility) if first else per_node(mobility),
    ]
    out_dims = [(picks, order, out_planes) + plane]
    if with_rates:
        out_dims.append((picks, order, out_planes - 2) + plane)
    out_shape = [jax.ShapeDtypeStruct(dims, jnp.float32) for dims in out_dims]
    out_specs = [per_out(dims) for dims in out_dims]
    scratch = [pltpu.VMEM((order, goal_planes) + plane, jnp.float32)]
    scratch += [pltpu.VMEM((order, goal_planes) + plane, jnp.float32) for _ in range(min(2, JACOBI - 1))]
    kernel = functools.partial(
        sweep_kernel, halo=halo, depth=depth, first=first, with_rates=with_rates, jacobi=JACOBI
    )
    result = pl.pallas_call(
        kernel,
        out_shape=tuple(out_shape),
        grid_spec=pltpu.PrefetchScalarGridSpec(
            num_scalar_prefetch=1,
            grid=(picks,),
            in_specs=in_specs,
            out_specs=tuple(out_specs),
            scratch_shapes=scratch,
        ),
        compiler_params=pltpu.CompilerParams(vmem_limit_bytes=60 * 1024 * 1024),
    )(sel, coef, state, rates, start, factor, mobility)
    return result


def on_device(grain_ids, peak_heat):
    total_nodes = lax.axis_size("node") * NODE_DEV
    node_times, table = radau_table(total_nodes)
    times = jnp.asarray(node_times, jnp.float32)
    taus = times.reshape((total_nodes, 1, 1, 1, 1, 1))
    coef = jnp.asarray(
        (time_step * table - time_step * np.diag(node_times)).astype(np.float32)
    )
    mine = lax.axis_index("node") * NODE_DEV
    depth = SWEEPS * JACOBI
    orders = jnp.arange(P_SIZE, dtype=jnp.int32)
    every = jnp.asarray(np.arange(total_nodes, dtype=np.int32))

    packed = jnp.stack([grain_ids.astype(jnp.float32), peak_heat])
    planes, rows, lanes = grain_ids.shape
    packed = packed.reshape((2, planes, rows // 2, 2, lanes)).transpose((0, 1, 3, 2, 4))
    packed = gather_halo(packed, 1, depth)
    ids_wide = packed[0]
    peak_wide = packed[1]
    start = (ids_wide[None] == orders[:, None, None, None, None].astype(jnp.float32)).astype(jnp.float32)

    states = None
    for step_index in range(STEPS):
        last_step = step_index + 1 == STEPS
        moments = (step_index + times) * time_step
        mobility = heat_mobility(peak_wide[None], moments[:, None, None, None, None])[:, None]
        factor = time_step * taus * mobility
        rates, pull = prep_call(start)
        halo = depth
        states = pull
        for sweep_index in range(SWEEPS):
            last = sweep_index + 1 == SWEEPS
            if last:
                keep = mine if last_step else total_nodes - 1
                if last_step:
                    sel = jnp.reshape(jnp.asarray(keep, jnp.int32), (1,))
                else:
                    sel = jnp.asarray(np.array([keep], np.int32))
            else:
                sel = every
            outs = sweep_call(
                sel, coef, states, rates, start, factor, mobility,
                halo, depth, sweep_index == 0, not last,
            )
            states = outs[0]
            if not last:
                rates = outs[1]
            halo -= JACOBI
        if not last_step:
            start = gather_halo(states[0], 1, depth)
    count, order, planes = states.shape[:3]
    return states.transpose((0, 1, 2, 4, 3, 5)).reshape((count, order, planes, rows, lanes))


def solution(mesh):
    in_specs = (P("space", None, None), P("space", None, None))
    out_specs = P("node", None, "space", None, None)
    return jax.shard_map(
        on_device, mesh=mesh, in_specs=in_specs, out_specs=out_specs, check_vma=False
    )
```
